128 devices in a mesh: shot: 16 (over y_lo, z, core), freq: 8 (over y_hi, x).
Axes of the slice: x: 4, y: 4 (y_hi: 2, y_lo: 2; y = y_hi * 2 + y_lo), z: 4, core: 2. Of those that a mesh axis runs over, the one named last changes fastest.
Arguments:
- traces: bfloat16 [1024, 1024, 512], P('shot', 'freq'), may hold values from -6 to 6
Outputs:
- multiples: bfloat16 [1024, 1024, 512], P('shot', 'freq')
The draws below stay inside these ranges and needn't reach their ends.
All inputs are finite; a program needn't handle non-finite values.
Results may differ from the reference program's by a relative error of at most 0.001.
Values sent between devices are 32-bit elements; how exact they have to be, the bound alone decides.
No kernel may reach another device: no remote copies, remote signals or barrier semaphores. Data moves between devices by JAX's collectives and lax.ppermute only.
A program may use at most 128 MiB of HBM per device.

```python
import jax
import jax.numpy as jnp
from jax import lax

SHOT_DEV = 64
NS = 1024
NT = 512
NF = 128
N_SHOT = 16


def block_scale(stream_key, extent, cuts, smallest, largest):
    gain, own = 1.0, jax.random.fold_in(stream_key, 6)
    for axis_at, blocks in cuts:
        heights = jnp.exp(jax.random.uniform(jax.random.fold_in(own, axis_at), (blocks,), jnp.float32, smallest / len(cuts), largest / len(cuts)))
        gain = gain * jnp.repeat(heights, extent[axis_at] // blocks).reshape([-1 if axis == axis_at else 1 for axis in range(len(extent))])
    return gain


def bell_draw(rng, extent, width, reach, split=(), kind=jnp.bfloat16):
    result = jax.random.normal(rng, extent, jnp.float32) * width
    if len(split) > 0:
        result = block_scale(rng, extent, split, -0.22, 0.18) * result
    return jnp.clip(result, min=-reach, max=reach).astype(kind)


def setup_inputs(seed: int = 0) -> dict:
    keys = jax.random.split(jax.random.key(seed), 2)
    return {
        "traces": bell_draw(keys[0], (NS, NS, NT), 1.0, 6.0, ((0, 16), (1, 8))),
    }


def make_tables(count_t, count_f):
    times = jnp.arange(count_t, dtype=jnp.int32)
    bins = count_t // 32 + jnp.arange(count_f, dtype=jnp.int32)
    phase = (times[:, None] * bins[None, :] % count_t).astype(jnp.float32) * (2.0 * jnp.pi / count_t)
    ramp = float(count_t // 16)
    tval = times.astype(jnp.float32)
    taper = jnp.minimum(jnp.minimum((tval + 0.5) / ramp, (count_t - tval - 0.5) / ramp), 1.0)
    cosine = jnp.cos(phase) * taper[:, None]
    sine = jnp.sin(phase) * taper[:, None]
    forward = jnp.stack([cosine, -sine], axis=1) / jnp.sqrt(jnp.float32(count_t))
    inverse = jnp.stack([cosine.T, -sine.T], axis=1) / jnp.sqrt(jnp.float32(count_f))
    return (forward, inverse)

def reference(traces):
    forward, inverse = make_tables(NT, NF)
    blocks = traces.reshape(N_SHOT, SHOT_DEV, NS, NT)

    def to_freq(block):
        return jnp.einsum('srt,tpb->bpsr', block.astype(jnp.float32), forward, precision=lax.Precision.HIGHEST, preferred_element_type=jnp.float32)
    spectra = jnp.moveaxis(lax.map(to_freq, blocks), 0, 2).reshape(NF, 2, NS, NS)

    def predict(spec):
        real, imag = (spec[0], spec[1])
        dot = lambda a, b: jnp.dot(a, b, precision=lax.Precision.HIGHEST, preferred_element_type=jnp.float32)
        return jnp.stack([dot(real, real) - dot(imag, imag), dot(real, imag) + dot(imag, real)], axis=0)
    pred = lax.map(predict, spectra) * (-1.0 / jnp.sqrt(jnp.float32(NS)))
    pred_blocks = jnp.moveaxis(pred.reshape(NF, 2, N_SHOT, SHOT_DEV, NS), 2, 0)

    def to_time(block):
        return jnp.einsum('bpsr,bpt->srt', block, inverse, precision=lax.Precision.HIGHEST, preferred_element_type=jnp.float32).astype(jnp.bfloat16)
    return lax.map(to_time, pred_blocks).reshape(NS, NS, NT)
```

```python
import jax
import jax.numpy as jnp
from jax import lax
from jax.sharding import PartitionSpec as P

NT = 512
NF = 128


def make_tables(count_t, count_f):
    times = jnp.arange(count_t, dtype=jnp.int32)
    bins = count_t // 32 + jnp.arange(count_f, dtype=jnp.int32)
    phase = (times[:, None] * bins[None, :] % count_t).astype(jnp.float32) * (
        2.0 * jnp.pi / count_t
    )
    ramp = float(count_t // 16)
    tval = times.astype(jnp.float32)
    taper = jnp.minimum(jnp.minimum((tval + 0.5) / ramp, (count_t - tval - 0.5) / ramp), 1.0)
    cosine = jnp.cos(phase) * taper[:, None]
    sine = jnp.sin(phase) * taper[:, None]
    forward = jnp.stack([cosine, -sine], axis=1) / jnp.sqrt(jnp.float32(count_t))
    inverse = jnp.stack([cosine.T, -sine.T], axis=1) / jnp.sqrt(jnp.float32(count_f))
    return (forward, inverse)


def batched_product(left, right):
    return jnp.einsum(
        "bsk,bkr->bsr",
        left,
        right,
        precision=lax.Precision.HIGH,
        preferred_element_type=jnp.float32,
    )


def complex_square(matrix):
    real, imag = (matrix[:, 0], matrix[:, 1])
    rr = batched_product(real, real)
    ii = batched_product(imag, imag)
    both = real + imag
    ss = batched_product(both, both)
    return jnp.stack([rr - ii, ss - rr - ii], axis=1)


def per_device(traces):
    forward, inverse = make_tables(NT, NF)
    spectra = jnp.einsum(
        "srt,tpb->bpsr",
        traces.astype(jnp.float32),
        forward,
        precision=lax.Precision.HIGH,
        preferred_element_type=jnp.float32,
    )
    rows = traces.shape[0]
    cols = traces.shape[1]
    n_shot = lax.axis_size("shot")
    n_freq = lax.axis_size("freq")
    moved = lax.all_to_all(spectra[None], ("shot", "freq"), split_axis=1, concat_axis=0, tiled=True)
    local_bins = moved.shape[-4]
    blocks = moved.reshape(n_shot, n_freq, local_bins, 2, rows, cols)
    matrix = blocks.transpose(2, 3, 0, 4, 1, 5).reshape(local_bins, 2, n_shot * rows, n_freq * cols)
    order = matrix.shape[2]
    pred = complex_square(matrix) * (-1.0 / jnp.sqrt(jnp.float32(order)))
    arranged = pred.reshape(local_bins, 2, n_shot, rows, n_freq, cols).transpose(2, 4, 0, 1, 3, 5)
    home = lax.all_to_all(
        arranged.reshape(n_shot * n_freq, local_bins, 2, rows, cols),
        ("shot", "freq"),
        split_axis=0,
        concat_axis=1,
        tiled=True,
    )
    home = home.reshape(n_shot * n_freq * local_bins, 2, rows, cols)
    result = jnp.einsum(
        "bpsr,bpt->srt",
        home,
        inverse,
        precision=lax.Precision.HIGH,
        preferred_element_type=jnp.float32,
    )
    return result.astype(jnp.bfloat16)


def solution(mesh):
    return jax.shard_map(
        per_device,
        mesh=mesh,
        in_specs=(P("shot", "freq", None),),
        out_specs=P("shot", "freq", None),
        check_vma=False,
    )
```

```python
import jax
import jax.numpy as jnp
from jax import lax
from jax.sharding import PartitionSpec as P

NT = 512
NF = 128


def make_tables(count_t, count_f):
    times = jnp.arange(count_t, dtype=jnp.int32)
    bins = count_t // 32 + jnp.arange(count_f, dtype=jnp.int32)
    phase = (times[:, None] * bins[None, :] % count_t).astype(jnp.float32) * (
        2.0 * jnp.pi / count_t
    )
    ramp = float(count_t // 16)
    tval = times.astype(jnp.float32)
    taper = jnp.minimum(jnp.minimum((tval + 0.5) / ramp, (count_t - tval - 0.5) / ramp), 1.0)
    cosine = jnp.cos(phase) * taper[:, None]
    sine = jnp.sin(phase) * taper[:, None]
    forward = jnp.stack([cosine, -sine], axis=1) / jnp.sqrt(jnp.float32(count_t))
    inverse = jnp.stack([cosine.T, -sine.T], axis=1) / jnp.sqrt(jnp.float32(count_f))
    return (forward, inverse)


def batched_product(left, right):
    return jnp.einsum(
        "bsk,bkr->bsr",
        left,
        right,
        precision=lax.Precision.HIGH,
        preferred_element_type=jnp.float32,
    )


def complex_square(matrix):
    real, imag = (matrix[:, 0], matrix[:, 1])
    rr = batched_product(real, real)
    ii = batched_product(imag, imag)
    both = real + imag
    ss = batched_product(both, both)
    return jnp.stack([rr - ii, ss - rr - ii], axis=1)


CHUNKS = 4


def dot(left, right):
    return jnp.dot(
        left, right, precision=lax.Precision.HIGH, preferred_element_type=jnp.float32
    )


def per_device(traces):
    forward, inverse = make_tables(NT, NF)
    spectra = jnp.einsum(
        "srt,tpb->bpsr",
        traces.astype(jnp.float32),
        forward,
        precision=lax.Precision.HIGH,
        preferred_element_type=jnp.float32,
    )
    rows = traces.shape[0]
    cols = traces.shape[1]
    n_shot = lax.axis_size("shot")
    n_freq = lax.axis_size("freq")
    moved = lax.all_to_all(spectra[None], ("shot", "freq"), split_axis=1, concat_axis=0, tiled=True)
    local_bins = moved.shape[-4]
    assert local_bins == 1
    blocks = moved.reshape(n_shot, n_freq, 2, rows, cols)
    order = n_shot * rows
    matrix = blocks.transpose(2, 0, 3, 1, 4).reshape(2, order, n_freq * cols)
    real, imag = matrix[0], matrix[1]
    both = real + imag
    scale = -1.0 / jnp.sqrt(jnp.float32(order))
    step = rows // CHUNKS
    outs = []
    for c in range(CHUNKS):
        def take(m):
            return m.reshape(n_shot, rows, -1)[:, c * step:(c + 1) * step].reshape(n_shot * step, -1)

        rr = dot(take(real), real)
        ii = dot(take(imag), imag)
        ss = dot(take(both), both)
        pred = jnp.stack([rr - ii, ss - rr - ii], axis=0) * scale
        arranged = pred.reshape(2, n_shot, step, n_freq, cols).transpose(1, 3, 0, 2, 4)
        home = lax.all_to_all(
            arranged.reshape(n_shot * n_freq, 1, 2, step, cols),
            ("shot", "freq"),
            split_axis=0,
            concat_axis=1,
            tiled=True,
        )
        home = home.reshape(n_shot * n_freq, 2, step, cols)
        result = jnp.einsum(
            "bpsr,bpt->srt",
            home,
            inverse,
            precision=lax.Precision.HIGH,
            preferred_element_type=jnp.float32,
        )
        outs.append(result.astype(jnp.bfloat16))
    return jnp.concatenate(outs, axis=0)


def solution(mesh):
    return jax.shard_map(
        per_device,
        mesh=mesh,
        in_specs=(P("shot", "freq", None),),
        out_specs=P("shot", "freq", None),
        check_vma=False,
    )
```

```python
import functools

import jax
import jax.numpy as jnp
from jax import lax
from jax.experimental import pallas as pl
from jax.experimental.pallas import tpu as pltpu
from jax.sharding import PartitionSpec as P

NT = 512
NF = 128


def make_tables(count_t, count_f):
    times = jnp.arange(count_t, dtype=jnp.int32)
    bins = count_t // 32 + jnp.arange(count_f, dtype=jnp.int32)
    phase = (times[:, None] * bins[None, :] % count_t).astype(jnp.float32) * (
        2.0 * jnp.pi / count_t
    )
    ramp = float(count_t // 16)
    tval = times.astype(jnp.float32)
    taper = jnp.minimum(jnp.minimum((tval + 0.5) / ramp, (count_t - tval - 0.5) / ramp), 1.0)
    cosine = jnp.cos(phase) * taper[:, None]
    sine = jnp.sin(phase) * taper[:, None]
    forward = jnp.stack([cosine, -sine], axis=1) / jnp.sqrt(jnp.float32(count_t))
    inverse = jnp.stack([cosine.T, -sine.T], axis=1) / jnp.sqrt(jnp.float32(count_f))
    return (forward, inverse)


def split(x):
    high = x.astype(jnp.bfloat16)
    low = (x - high.astype(jnp.float32)).astype(jnp.bfloat16)
    return high, low


def product(high, low, left, right):
    dot = functools.partial(jnp.dot, preferred_element_type=jnp.float32)
    return (
        dot(high[left], high[right])
        + dot(high[left], low[right])
        + dot(low[left], high[right])
    )


def square_kernel(n_shot, n_freq, rows, cols, scale, y_ref, out_ref, high, low):
    width = out_ref.shape[1] * cols
    j = pl.program_id(0)

    @pl.when(j == 0)
    def _():
        def fill(a, carry):
            top = pl.multiple_of(a * rows, rows)
            for b in range(n_freq):
                real = y_ref[a, b, 0]
                imag = y_ref[a, b, 1]
                for index, part in enumerate((real, imag, real + imag)):
                    h, l = split(part)
                    high[index, pl.ds(top, rows), pl.ds(b * cols, cols)] = h
                    low[index, pl.ds(top, rows), pl.ds(b * cols, cols)] = l
            return carry

        lax.fori_loop(0, n_shot, fill, 0)

    start = pl.multiple_of(j * width, width)
    every = slice(None)
    block = pl.ds(start, width)

    def side(index):
        return (index, every, every), (index, every, block)

    rr = product(high, low, *side(0))
    ii = product(high, low, *side(1))
    ss = product(high, low, *side(2))
    real = (rr - ii) * scale
    imag = (ss - rr - ii) * scale
    for a in range(n_shot):
        for b in range(out_ref.shape[1]):
            tile = (slice(a * rows, (a + 1) * rows), slice(b * cols, (b + 1) * cols))
            out_ref[a, b, 0] = real[tile]
            out_ref[a, b, 1] = imag[tile]


def complex_square(blocks):
    n_shot, n_freq, _, rows, cols = blocks.shape
    order = n_shot * rows
    group = 2
    kernel = functools.partial(
        square_kernel, n_shot, n_freq, rows, cols, float(-1.0 / (order ** 0.5))
    )
    return pl.pallas_call(
        kernel,
        out_shape=jax.ShapeDtypeStruct(blocks.shape, jnp.float32),
        grid=(n_freq // group,),
        in_specs=[pl.BlockSpec(memory_space=pltpu.VMEM)],
        out_specs=pl.BlockSpec(
            (n_shot, group, 2, rows, cols), lambda j: (0, j, 0, 0, 0)
        ),
        scratch_shapes=[
            pltpu.VMEM((3, order, n_freq * cols), jnp.bfloat16),
            pltpu.VMEM((3, order, n_freq * cols), jnp.bfloat16),
        ],
        compiler_params=pltpu.CompilerParams(
            dimension_semantics=("arbitrary",), vmem_limit_bytes=60 * 1024 * 1024
        ),
    )(blocks)


def per_device(traces):
    forward, inverse = make_tables(NT, NF)
    spectra = jnp.einsum(
        "srt,tpb->bpsr",
        traces.astype(jnp.float32),
        forward,
        precision=lax.Precision.HIGH,
        preferred_element_type=jnp.float32,
    )
    rows = traces.shape[0]
    cols = traces.shape[1]
    n_shot = lax.axis_size("shot")
    n_freq = lax.axis_size("freq")
    moved = lax.all_to_all(spectra[None], ("shot", "freq"), split_axis=1, concat_axis=0, tiled=True)
    local_bins = moved.shape[-4]
    assert local_bins == 1
    blocks = moved.reshape(n_shot, n_freq, 2, rows, cols)
    pred = complex_square(blocks)
    home = lax.all_to_all(
        pred.reshape(n_shot * n_freq, 1, 2, rows, cols),
        ("shot", "freq"),
        split_axis=0,
        concat_axis=1,
        tiled=True,
    )
    home = home.reshape(n_shot * n_freq, 2, rows, cols)
    result = jnp.einsum(
        "bpsr,bpt->srt",
        home,
        inverse,
        precision=lax.Precision.HIGH,
        preferred_element_type=jnp.float32,
    )
    return result.astype(jnp.bfloat16)


def solution(mesh):
    return jax.shard_map(
        per_device,
        mesh=mesh,
        in_specs=(P("shot", "freq", None),),
        out_specs=P("shot", "freq", None),
        check_vma=False,
    )
```

```python
import functools

import jax
import jax.numpy as jnp
from jax import lax
from jax.experimental import pallas as pl
from jax.experimental.pallas import tpu as pltpu
from jax.sharding import PartitionSpec as P

NT = 512
NF = 128


def make_tables(count_t, count_f):
    times = jnp.arange(count_t, dtype=jnp.int32)
    bins = count_t // 32 + jnp.arange(count_f, dtype=jnp.int32)
    phase = (times[:, None] * bins[None, :] % count_t).astype(jnp.float32) * (
        2.0 * jnp.pi / count_t
    )
    ramp = float(count_t // 16)
    tval = times.astype(jnp.float32)
    taper = jnp.minimum(jnp.minimum((tval + 0.5) / ramp, (count_t - tval - 0.5) / ramp), 1.0)
    cosine = jnp.cos(phase) * taper[:, None]
    sine = jnp.sin(phase) * taper[:, None]
    forward = jnp.stack([cosine, -sine], axis=1) / jnp.sqrt(jnp.float32(count_t))
    inverse = jnp.stack([cosine.T, -sine.T], axis=1) / jnp.sqrt(jnp.float32(count_f))
    return (forward, inverse)


def split(x):
    high = x.astype(jnp.bfloat16)
    low = (x - high.astype(jnp.float32)).astype(jnp.bfloat16)
    return high, low


def split_outside(x):
    high = lax.reduce_precision(x, exponent_bits=8, mantissa_bits=7)
    return high.astype(jnp.bfloat16), (x - high).astype(jnp.bfloat16)


def product(high, low, left, right):
    dot = functools.partial(jnp.dot, preferred_element_type=jnp.float32)
    return (
        dot(high[left], high[right])
        + dot(high[left], low[right])
        + dot(low[left], high[right])
    )


def square_kernel(n_shot, n_freq, rows, cols, scale, y_ref, out_ref, high, low):
    width = out_ref.shape[1] * cols
    j = pl.program_id(0)

    @pl.when(j == 0)
    def _():
        def fill(a, carry):
            top = pl.multiple_of(a * rows, rows)
            for b in range(n_freq):
                real = y_ref[a, b, 0]
                imag = y_ref[a, b, 1]
                for index, part in enumerate((real, imag, real + imag)):
                    h, l = split(part)
                    high[index, pl.ds(top, rows), pl.ds(b * cols, cols)] = h
                    low[index, pl.ds(top, rows), pl.ds(b * cols, cols)] = l
            return carry

        lax.fori_loop(0, n_shot, fill, 0)

    start = pl.multiple_of(j * width, width)
    every = slice(None)
    block = pl.ds(start, width)

    def side(index):
        return (index, every, every), (index, every, block)

    rr = product(high, low, *side(0))
    ii = product(high, low, *side(1))
    ss = product(high, low, *side(2))
    real = (rr - ii) * scale
    imag = (ss - rr - ii) * scale
    for a in range(n_shot):
        for b in range(out_ref.shape[1]):
            tile = (slice(a * rows, (a + 1) * rows), slice(b * cols, (b + 1) * cols))
            out_ref[a, b, 0] = real[tile]
            out_ref[a, b, 1] = imag[tile]


def complex_square(blocks):
    n_shot, n_freq, _, rows, cols = blocks.shape
    order = n_shot * rows
    group = 2
    kernel = functools.partial(
        square_kernel, n_shot, n_freq, rows, cols, float(-1.0 / (order ** 0.5))
    )
    return pl.pallas_call(
        kernel,
        out_shape=jax.ShapeDtypeStruct(blocks.shape, jnp.float32),
        grid=(n_freq // group,),
        in_specs=[pl.BlockSpec(memory_space=pltpu.VMEM)],
        out_specs=pl.BlockSpec(
            (n_shot, group, 2, rows, cols), lambda j: (0, j, 0, 0, 0)
        ),
        scratch_shapes=[
            pltpu.VMEM((3, order, n_freq * cols), jnp.bfloat16),
            pltpu.VMEM((3, order, n_freq * cols), jnp.bfloat16),
        ],
        compiler_params=pltpu.CompilerParams(
            dimension_semantics=("arbitrary",), vmem_limit_bytes=60 * 1024 * 1024
        ),
    )(blocks)


def inverse_kernel(group, w_high, w_low, x_ref, out_ref):
    n_bins, parts, _, cols = x_ref.shape
    pieces = []
    for s in range(group):
        piece = x_ref[:, :, s, :].reshape(n_bins * parts, cols)
        pieces.append(piece.T)
    stacked = jnp.concatenate(pieces, axis=0)
    high, low = split(stacked)
    dot = functools.partial(jnp.dot, preferred_element_type=jnp.float32)
    total = dot(high, w_high[...]) + dot(high, w_low[...]) + dot(low, w_high[...])
    out_ref[...] = total.reshape(out_ref.shape).astype(out_ref.dtype)


def inverse_transform(home, inverse):
    n_bins, parts, rows, cols = home.shape
    steps = inverse.shape[-1]
    table = inverse.reshape(n_bins * parts, steps)
    w_high, w_low = split_outside(table)
    group = 8
    return pl.pallas_call(
        functools.partial(inverse_kernel, group),
        out_shape=jax.ShapeDtypeStruct((rows, cols, steps), jnp.bfloat16),
        grid=(rows // group,),
        in_specs=[
            pl.BlockSpec((n_bins * parts, steps), lambda i: (0, 0)),
            pl.BlockSpec((n_bins * parts, steps), lambda i: (0, 0)),
            pl.BlockSpec((n_bins, parts, group, cols), lambda i: (0, 0, i, 0)),
        ],
        out_specs=pl.BlockSpec((group, cols, steps), lambda i: (i, 0, 0)),
        compiler_params=pltpu.CompilerParams(dimension_semantics=("arbitrary",)),
    )(w_high, w_low, home)


def per_device(traces):
    forward, inverse = make_tables(NT, NF)
    spectra = jnp.einsum(
        "srt,tpb->bpsr",
        traces.astype(jnp.float32),
        forward,
        precision=lax.Precision.HIGH,
        preferred_element_type=jnp.float32,
    )
    rows = traces.shape[0]
    cols = traces.shape[1]
    n_shot = lax.axis_size("shot")
    n_freq = lax.axis_size("freq")
    moved = lax.all_to_all(spectra[None], ("shot", "freq"), split_axis=1, concat_axis=0, tiled=True)
    local_bins = moved.shape[-4]
    assert local_bins == 1
    blocks = moved.reshape(n_shot, n_freq, 2, rows, cols)
    pred = complex_square(blocks)
    home = lax.all_to_all(
        pred.reshape(1, n_shot * n_freq, 2, rows, cols),
        ("shot", "freq"),
        split_axis=1,
        concat_axis=0,
        tiled=True,
    )
    home = home.reshape(n_shot * n_freq, 2, rows, cols)
    return inverse_transform(home, inverse)


def solution(mesh):
    return jax.shard_map(
        per_device,
        mesh=mesh,
        in_specs=(P("shot", "freq", None),),
        out_specs=P("shot", "freq", None),
        check_vma=False,
    )
```

```python
import functools

import jax
import jax.numpy as jnp
from jax import lax
from jax.experimental import pallas as pl
from jax.experimental.pallas import tpu as pltpu
from jax.sharding import PartitionSpec as P

NT = 512
NF = 128


def make_tables(count_t, count_f):
    times = jnp.arange(count_t, dtype=jnp.int32)
    bins = count_t // 32 + jnp.arange(count_f, dtype=jnp.int32)
    phase = (times[:, None] * bins[None, :] % count_t).astype(jnp.float32) * (
        2.0 * jnp.pi / count_t
    )
    ramp = float(count_t // 16)
    tval = times.astype(jnp.float32)
    taper = jnp.minimum(jnp.minimum((tval + 0.5) / ramp, (count_t - tval - 0.5) / ramp), 1.0)
    cosine = jnp.cos(phase) * taper[:, None]
    sine = jnp.sin(phase) * taper[:, None]
    forward = jnp.stack([cosine, -sine], axis=1) / jnp.sqrt(jnp.float32(count_t))
    inverse = jnp.stack([cosine.T, -sine.T], axis=1) / jnp.sqrt(jnp.float32(count_f))
    return (forward, inverse)


def split(x):
    high = x.astype(jnp.bfloat16)
    low = (x - high.astype(jnp.float32)).astype(jnp.bfloat16)
    return high, low


def split_outside(x):
    high = lax.reduce_precision(x, exponent_bits=8, mantissa_bits=7)
    return high.astype(jnp.bfloat16), (x - high).astype(jnp.bfloat16)


def product(high, low, left, right):
    dot = functools.partial(jnp.dot, preferred_element_type=jnp.float32)
    return (
        dot(high[left], high[right])
        + dot(high[left], low[right])
        + dot(low[left], high[right])
    )


def square_kernel(n_shot, n_freq, rows, cols, scale, y_ref, out_ref, high, low):
    width = out_ref.shape[1] * cols
    j = pl.program_id(0)

    @pl.when(j == 0)
    def _():
        def fill(a, carry):
            top = pl.multiple_of(a * rows, rows)
            for b in range(n_freq):
                real = y_ref[a, b, 0]
                imag = y_ref[a, b, 1]
                for index, part in enumerate((real, imag, real + imag)):
                    h, l = split(part)
                    high[index, pl.ds(top, rows), pl.ds(b * cols, cols)] = h
                    low[index, pl.ds(top, rows), pl.ds(b * cols, cols)] = l
            return carry

        lax.fori_loop(0, n_shot, fill, 0)

    start = pl.multiple_of(j * width, width)
    every = slice(None)
    block = pl.ds(start, width)

    def side(index):
        return (index, every, every), (index, every, block)

    rr = product(high, low, *side(0))
    ii = product(high, low, *side(1))
    ss = product(high, low, *side(2))
    real = (rr - ii) * scale
    imag = (ss - rr - ii) * scale
    for a in range(n_shot):
        for b in range(out_ref.shape[1]):
            tile = (slice(a * rows, (a + 1) * rows), slice(b * cols, (b + 1) * cols))
            out_ref[a, b, 0] = real[tile]
            out_ref[a, b, 1] = imag[tile]


def complex_square(blocks):
    n_shot, n_freq, _, rows, cols = blocks.shape
    order = n_shot * rows
    group = 2
    kernel = functools.partial(
        square_kernel, n_shot, n_freq, rows, cols, float(-1.0 / (order ** 0.5))
    )
    return pl.pallas_call(
        kernel,
        out_shape=jax.ShapeDtypeStruct(blocks.shape, jnp.float32),
        grid=(n_freq // group,),
        in_specs=[pl.BlockSpec(memory_space=pltpu.VMEM)],
        out_specs=pl.BlockSpec(
            (n_shot, group, 2, rows, cols), lambda j: (0, j, 0, 0, 0)
        ),
        scratch_shapes=[
            pltpu.VMEM((3, order, n_freq * cols), jnp.bfloat16),
            pltpu.VMEM((3, order, n_freq * cols), jnp.bfloat16),
        ],
        compiler_params=pltpu.CompilerParams(
            dimension_semantics=("arbitrary",), vmem_limit_bytes=60 * 1024 * 1024
        ),
    )(blocks)


def inverse_kernel(group, w_high, w_low, x_ref, out_ref):
    n_bins, parts, _, cols = x_ref.shape
    pieces = []
    for s in range(group):
        piece = x_ref[:, :, s, :].reshape(n_bins * parts, cols)
        pieces.append(piece.T)
    stacked = jnp.concatenate(pieces, axis=0)
    high, low = split(stacked)
    dot = functools.partial(jnp.dot, preferred_element_type=jnp.float32)
    total = dot(high, w_high[...]) + dot(high, w_low[...]) + dot(low, w_high[...])
    out_ref[...] = total.reshape(out_ref.shape).astype(out_ref.dtype)


def inverse_transform(home, inverse):
    n_bins, parts, rows, cols = home.shape
    steps = inverse.shape[-1]
    table = inverse.reshape(n_bins * parts, steps)
    w_high, w_low = split_outside(table)
    group = 8
    return pl.pallas_call(
        functools.partial(inverse_kernel, group),
        out_shape=jax.ShapeDtypeStruct((rows, cols, steps), jnp.bfloat16),
        grid=(rows // group,),
        in_specs=[
            pl.BlockSpec((n_bins * parts, steps), lambda i: (0, 0)),
            pl.BlockSpec((n_bins * parts, steps), lambda i: (0, 0)),
            pl.BlockSpec((n_bins, parts, group, cols), lambda i: (0, 0, i, 0)),
        ],
        out_specs=pl.BlockSpec((group, cols, steps), lambda i: (i, 0, 0)),
        compiler_params=pltpu.CompilerParams(dimension_semantics=("arbitrary",)),
    )(w_high, w_low, home)


def forward_kernel(group, w_high, w_low, x_ref, out_ref):
    _, cols, steps = x_ref.shape
    flat = x_ref[...].reshape(group * cols, steps)
    dims = (((1,), (1,)), ((), ()))
    dot = functools.partial(lax.dot_general, dimension_numbers=dims, preferred_element_type=jnp.float32)
    total = dot(w_high[...], flat) + dot(w_low[...], flat)
    n_bins, parts = out_ref.shape[0], out_ref.shape[1]
    for s in range(group):
        piece = total[:, s * cols:(s + 1) * cols].reshape(n_bins, parts, cols)
        out_ref[:, :, s, :] = piece


def forward_transform(traces, forward):
    rows, cols, steps = traces.shape
    parts, n_bins = forward.shape[1], forward.shape[2]
    table = forward.transpose(2, 1, 0).reshape(n_bins * parts, steps)
    w_high, w_low = split_outside(table)
    group = 8
    return pl.pallas_call(
        functools.partial(forward_kernel, group),
        out_shape=jax.ShapeDtypeStruct((n_bins, parts, rows, cols), jnp.float32),
        grid=(rows // group,),
        in_specs=[
            pl.BlockSpec((n_bins * parts, steps), lambda i: (0, 0)),
            pl.BlockSpec((n_bins * parts, steps), lambda i: (0, 0)),
            pl.BlockSpec((group, cols, steps), lambda i: (i, 0, 0)),
        ],
        out_specs=pl.BlockSpec((n_bins, parts, group, cols), lambda i: (0, 0, i, 0)),
        compiler_params=pltpu.CompilerParams(dimension_semantics=("arbitrary",)),
    )(w_high, w_low, traces)


def per_device(traces):
    forward, inverse = make_tables(NT, NF)
    spectra = forward_transform(traces, forward)
    rows = traces.shape[0]
    cols = traces.shape[1]
    n_shot = lax.axis_size("shot")
    n_freq = lax.axis_size("freq")
    moved = lax.all_to_all(spectra[None], ("shot", "freq"), split_axis=1, concat_axis=0, tiled=True)
    local_bins = moved.shape[-4]
    assert local_bins == 1
    blocks = moved.reshape(n_shot, n_freq, 2, rows, cols)
    pred = complex_square(blocks)
    home = lax.all_to_all(
        pred.reshape(1, n_shot * n_freq, 2, rows, cols),
        ("shot", "freq"),
        split_axis=1,
        concat_axis=0,
        tiled=True,
    )
    home = home.reshape(n_shot * n_freq, 2, rows, cols)
    return inverse_transform(home, inverse)


def solution(mesh):
    return jax.shard_map(
        per_device,
        mesh=mesh,
        in_specs=(P("shot", "freq", None),),
        out_specs=P("shot", "freq", None),
        check_vma=False,
    )
```

```python
import functools

import jax
import jax.numpy as jnp
from jax import lax
from jax.experimental import pallas as pl
from jax.experimental.pallas import tpu as pltpu
from jax.sharding import PartitionSpec as P

NT = 512
NF = 128
PARTS = 2


def make_tables(count_t, count_f):
    times = jnp.arange(count_t, dtype=jnp.int32)
    bins = count_t // 32 + jnp.arange(count_f, dtype=jnp.int32)
    phase = (times[:, None] * bins[None, :] % count_t).astype(jnp.float32) * (
        2.0 * jnp.pi / count_t
    )
    ramp = float(count_t // 16)
    tval = times.astype(jnp.float32)
    taper = jnp.minimum(jnp.minimum((tval + 0.5) / ramp, (count_t - tval - 0.5) / ramp), 1.0)
    cosine = jnp.cos(phase) * taper[:, None]
    sine = jnp.sin(phase) * taper[:, None]
    forward = jnp.stack([cosine, -sine], axis=1) / jnp.sqrt(jnp.float32(count_t))
    inverse = jnp.stack([cosine.T, -sine.T], axis=1) / jnp.sqrt(jnp.float32(count_f))
    return (forward, inverse)


def split(x):
    high = x.astype(jnp.bfloat16)
    low = (x - high.astype(jnp.float32)).astype(jnp.bfloat16)
    return high, low


def split_outside(x):
    high = lax.reduce_precision(x, exponent_bits=8, mantissa_bits=7)
    return high.astype(jnp.bfloat16), (x - high).astype(jnp.bfloat16)


def square_kernel(n_shot, n_freq, rows, cols, scale, part, y_ref, out_ref, high, low):
    width = out_ref.shape[1] * cols
    span = out_ref.shape[3]
    j = pl.program_id(0)

    @pl.when(j == 0)
    def _():
        def fill(a, carry):
            top = pl.multiple_of(a * rows, rows)
            for b in range(n_freq):
                real = y_ref[a, b, 0]
                imag = y_ref[a, b, 1]
                for index, value in enumerate((real, imag, real + imag)):
                    h, l = split(value)
                    high[index, pl.ds(top, rows), pl.ds(b * cols, cols)] = h
                    low[index, pl.ds(top, rows), pl.ds(b * cols, cols)] = l
            return carry

        lax.fori_loop(0, n_shot, fill, 0)

    start = pl.multiple_of(j * width, width)
    block = pl.ds(start, width)
    dot = functools.partial(jnp.dot, preferred_element_type=jnp.float32)

    def product(index):
        def left(ref):
            return jnp.concatenate(
                [ref[index, pl.ds(a * rows + part * span, span), :] for a in range(n_shot)],
                axis=0,
            )

        lh, ll = left(high), left(low)
        rh, rl = high[index, :, block], low[index, :, block]
        return dot(lh, rh) + dot(lh, rl) + dot(ll, rh)

    rr = product(0)
    ii = product(1)
    ss = product(2)
    real = (rr - ii) * scale
    imag = (ss - rr - ii) * scale
    for a in range(n_shot):
        for b in range(out_ref.shape[1]):
            tile = (slice(a * span, (a + 1) * span), slice(b * cols, (b + 1) * cols))
            out_ref[a, b, 0] = real[tile]
            out_ref[a, b, 1] = imag[tile]


def complex_square(blocks, part, parts):
    n_shot, n_freq, _, rows, cols = blocks.shape
    order = n_shot * rows
    span = rows // parts
    group = 2
    kernel = functools.partial(
        square_kernel, n_shot, n_freq, rows, cols, float(-1.0 / (order ** 0.5)), part
    )
    return pl.pallas_call(
        kernel,
        out_shape=jax.ShapeDtypeStruct((n_shot, n_freq, 2, span, cols), jnp.float32),
        grid=(n_freq // group,),
        in_specs=[pl.BlockSpec(memory_space=pltpu.VMEM)],
        out_specs=pl.BlockSpec(
            (n_shot, group, 2, span, cols), lambda j: (0, j, 0, 0, 0)
        ),
        scratch_shapes=[
            pltpu.VMEM((3, order, n_freq * cols), jnp.bfloat16),
            pltpu.VMEM((3, order, n_freq * cols), jnp.bfloat16),
        ],
        compiler_params=pltpu.CompilerParams(
            dimension_semantics=("arbitrary",), vmem_limit_bytes=60 * 1024 * 1024
        ),
    )(blocks)


def inverse_kernel(group, w_high, w_low, x_ref, out_ref):
    n_bins, parts, _, cols = x_ref.shape
    pieces = []
    for s in range(group):
        piece = x_ref[:, :, s, :].reshape(n_bins * parts, cols)
        pieces.append(piece.T)
    stacked = jnp.concatenate(pieces, axis=0)
    high, low = split(stacked)
    dot = functools.partial(jnp.dot, preferred_element_type=jnp.float32)
    total = dot(high, w_high[...]) + dot(high, w_low[...]) + dot(low, w_high[...])
    out_ref[...] = total.reshape(out_ref.shape).astype(out_ref.dtype)


def inverse_transform(home, inverse, part, parts, previous):
    n_bins, _, span, cols = home.shape
    steps = inverse.shape[-1]
    table = inverse.reshape(n_bins * 2, steps)
    w_high, w_low = split_outside(table)
    group = 8
    offset = part * (span // group)
    operands = [w_high, w_low, home]
    in_specs = [
        pl.BlockSpec((n_bins * 2, steps), lambda i: (0, 0)),
        pl.BlockSpec((n_bins * 2, steps), lambda i: (0, 0)),
        pl.BlockSpec((n_bins, 2, group, cols), lambda i: (0, 0, i, 0)),
    ]
    aliases = {}
    kernel = functools.partial(inverse_kernel, group)
    if previous is not None:
        operands.append(previous)
        in_specs.append(pl.BlockSpec(memory_space=pl.ANY))
        aliases = {3: 0}
        kernel = functools.partial(inverse_kernel_into, group)
    return pl.pallas_call(
        kernel,
        out_shape=jax.ShapeDtypeStruct((span * parts, cols, steps), jnp.bfloat16),
        grid=(span // group,),
        in_specs=in_specs,
        out_specs=pl.BlockSpec((group, cols, steps), lambda i: (i + offset, 0, 0)),
        input_output_aliases=aliases,
        compiler_params=pltpu.CompilerParams(dimension_semantics=("arbitrary",)),
    )(*operands)


def inverse_kernel_into(group, w_high, w_low, x_ref, previous_ref, out_ref):
    inverse_kernel(group, w_high, w_low, x_ref, out_ref)


def per_device(traces):
    forward, inverse = make_tables(NT, NF)
    spectra = jnp.einsum(
        "srt,tpb->bpsr",
        traces.astype(jnp.float32),
        forward,
        precision=lax.Precision.HIGH,
        preferred_element_type=jnp.float32,
    )
    rows = traces.shape[0]
    cols = traces.shape[1]
    n_shot = lax.axis_size("shot")
    n_freq = lax.axis_size("freq")
    moved = lax.all_to_all(spectra[None], ("shot", "freq"), split_axis=1, concat_axis=0, tiled=True)
    local_bins = moved.shape[-4]
    assert local_bins == 1
    blocks = moved.reshape(n_shot, n_freq, 2, rows, cols)
    result = None
    for part in range(PARTS):
        pred = complex_square(blocks, part, PARTS)
        span = pred.shape[3]
        home = lax.all_to_all(
            pred.reshape(1, n_shot * n_freq, 2, span, cols),
            ("shot", "freq"),
            split_axis=1,
            concat_axis=0,
            tiled=True,
        )
        home = home.reshape(n_shot * n_freq, 2, span, cols)
        result = inverse_transform(home, inverse, part, PARTS, result)
    return result


def solution(mesh):
    return jax.shard_map(
        per_device,
        mesh=mesh,
        in_specs=(P("shot", "freq", None),),
        out_specs=P("shot", "freq", None),
        check_vma=False,
    )
```

```python
import functools

import jax
import jax.numpy as jnp
from jax import lax
from jax.experimental import pallas as pl
from jax.experimental.pallas import tpu as pltpu
from jax.sharding import PartitionSpec as P

NT = 512
NF = 128
SPANS = (24, 40)


def make_tables(count_t, count_f):
    times = jnp.arange(count_t, dtype=jnp.int32)
    bins = count_t // 32 + jnp.arange(count_f, dtype=jnp.int32)
    phase = (times[:, None] * bins[None, :] % count_t).astype(jnp.float32) * (
        2.0 * jnp.pi / count_t
    )
    ramp = float(count_t // 16)
    tval = times.astype(jnp.float32)
    taper = jnp.minimum(jnp.minimum((tval + 0.5) / ramp, (count_t - tval - 0.5) / ramp), 1.0)
    cosine = jnp.cos(phase) * taper[:, None]
    sine = jnp.sin(phase) * taper[:, None]
    forward = jnp.stack([cosine, -sine], axis=1) / jnp.sqrt(jnp.float32(count_t))
    inverse = jnp.stack([cosine.T, -sine.T], axis=1) / jnp.sqrt(jnp.float32(count_f))
    return (forward, inverse)


def split(x):
    high = x.astype(jnp.bfloat16)
    low = (x - high.astype(jnp.float32)).astype(jnp.bfloat16)
    return high, low


def split_outside(x):
    high = lax.reduce_precision(x, exponent_bits=8, mantissa_bits=7)
    return high.astype(jnp.bfloat16), (x - high).astype(jnp.bfloat16)


def square_kernel(n_shot, n_freq, rows, cols, scale, first, y_hbm, out_ref, y_ref, sems, high, low):
    width = out_ref.shape[1] * cols
    span = out_ref.shape[3]
    j = pl.program_id(0)

    def copy(a):
        return pltpu.make_async_copy(y_hbm.at[a], y_ref.at[a], sems.at[a])

    @pl.when(j == 0)
    def _():
        for a in range(n_shot):
            copy(a).start()

        def fill(a, carry):
            copy(a).wait()
            top = pl.multiple_of(a * rows, rows)
            for b in range(n_freq):
                real = y_ref[a, b, 0]
                imag = y_ref[a, b, 1]
                for index, value in enumerate((real, imag, real + imag)):
                    h, l = split(value)
                    high[index, pl.ds(top, rows), pl.ds(b * cols, cols)] = h
                    low[index, pl.ds(top, rows), pl.ds(b * cols, cols)] = l
            return carry

        lax.fori_loop(0, n_shot, fill, 0)

    start = pl.multiple_of(j * width, width)
    block = pl.ds(start, width)
    dot = functools.partial(jnp.dot, preferred_element_type=jnp.float32)

    def product(index):
        def left(ref):
            return jnp.concatenate(
                [ref[index, pl.ds(a * rows + first, span), :] for a in range(n_shot)],
                axis=0,
            )

        lh, ll = left(high), left(low)
        rh, rl = high[index, :, block], low[index, :, block]
        return dot(lh, rh) + dot(lh, rl) + dot(ll, rh)

    rr = product(0)
    ii = product(1)
    ss = product(2)
    real = (rr - ii) * scale
    imag = (ss - rr - ii) * scale
    for a in range(n_shot):
        for b in range(out_ref.shape[1]):
            tile = (slice(a * span, (a + 1) * span), slice(b * cols, (b + 1) * cols))
            out_ref[a, b, 0] = real[tile]
            out_ref[a, b, 1] = imag[tile]


def complex_square(blocks, first, span):
    n_shot, n_freq, _, rows, cols = blocks.shape
    order = n_shot * rows
    group = 2
    kernel = functools.partial(
        square_kernel, n_shot, n_freq, rows, cols, float(-1.0 / (order ** 0.5)), first
    )
    return pl.pallas_call(
        kernel,
        out_shape=jax.ShapeDtypeStruct((n_shot, n_freq, 2, span, cols), jnp.float32),
        grid=(n_freq // group,),
        in_specs=[pl.BlockSpec(memory_space=pl.ANY)],
        out_specs=pl.BlockSpec(
            (n_shot, group, 2, span, cols), lambda j: (0, j, 0, 0, 0)
        ),
        scratch_shapes=[
            pltpu.VMEM(blocks.shape, jnp.float32),
            pltpu.SemaphoreType.DMA((n_shot,)),
            pltpu.VMEM((3, order, n_freq * cols), jnp.bfloat16),
            pltpu.VMEM((3, order, n_freq * cols), jnp.bfloat16),
        ],
        compiler_params=pltpu.CompilerParams(
            dimension_semantics=("arbitrary",), vmem_limit_bytes=60 * 1024 * 1024
        ),
    )(blocks)


def inverse_kernel(group, w_high, w_low, x_ref, out_ref):
    n_bins, parts, _, cols = x_ref.shape
    pieces = []
    for s in range(group):
        piece = x_ref[:, :, s, :].reshape(n_bins * parts, cols)
        pieces.append(piece.T)
    stacked = jnp.concatenate(pieces, axis=0)
    high, low = split(stacked)
    dot = functools.partial(jnp.dot, preferred_element_type=jnp.float32)
    total = dot(high, w_high[...]) + dot(high, w_low[...]) + dot(low, w_high[...])
    out_ref[...] = total.reshape(out_ref.shape).astype(out_ref.dtype)


def inverse_transform(home, inverse, first, total, previous):
    n_bins, _, span, cols = home.shape
    steps = inverse.shape[-1]
    table = inverse.reshape(n_bins * 2, steps)
    w_high, w_low = split_outside(table)
    group = 8
    offset = first // group
    operands = [w_high, w_low, home]
    in_specs = [
        pl.BlockSpec((n_bins * 2, steps), lambda i: (0, 0)),
        pl.BlockSpec((n_bins * 2, steps), lambda i: (0, 0)),
        pl.BlockSpec((n_bins, 2, group, cols), lambda i: (0, 0, i, 0)),
    ]
    aliases = {}
    kernel = functools.partial(inverse_kernel, group)
    if previous is not None:
        operands.append(previous)
        in_specs.append(pl.BlockSpec(memory_space=pl.ANY))
        aliases = {3: 0}
        kernel = functools.partial(inverse_kernel_into, group)
    return pl.pallas_call(
        kernel,
        out_shape=jax.ShapeDtypeStruct((total, cols, steps), jnp.bfloat16),
        grid=(span // group,),
        in_specs=in_specs,
        out_specs=pl.BlockSpec((group, cols, steps), lambda i: (i + offset, 0, 0)),
        input_output_aliases=aliases,
        compiler_params=pltpu.CompilerParams(dimension_semantics=("arbitrary",)),
    )(*operands)


def inverse_kernel_into(group, w_high, w_low, x_ref, previous_ref, out_ref):
    inverse_kernel(group, w_high, w_low, x_ref, out_ref)


def per_device(traces):
    forward, inverse = make_tables(NT, NF)
    spectra = jnp.einsum(
        "srt,tpb->bpsr",
        traces.astype(jnp.float32),
        forward,
        precision=lax.Precision.HIGH,
        preferred_element_type=jnp.float32,
    )
    rows = traces.shape[0]
    cols = traces.shape[1]
    n_shot = lax.axis_size("shot")
    n_freq = lax.axis_size("freq")
    moved = lax.all_to_all(spectra[None], ("shot", "freq"), split_axis=1, concat_axis=0, tiled=True)
    local_bins = moved.shape[-4]
    assert local_bins == 1
    blocks = moved.reshape(n_shot, n_freq, 2, rows, cols)
    result = None
    first = 0
    for span in SPANS:
        pred = complex_square(blocks, first, span)
        home = lax.all_to_all(
            pred.reshape(1, n_shot * n_freq, 2, span, cols),
            ("shot", "freq"),
            split_axis=1,
            concat_axis=0,
            tiled=True,
        )
        home = home.reshape(n_shot * n_freq, 2, span, cols)
        result = inverse_transform(home, inverse, first, rows, result)
        first += span
    assert first == rows
    return result


def solution(mesh):
    return jax.shard_map(
        per_device,
        mesh=mesh,
        in_specs=(P("shot", "freq", None),),
        out_specs=P("shot", "freq", None),
        check_vma=False,
    )
```

```python
import functools

import jax
import jax.numpy as jnp
from jax import lax
from jax.experimental import pallas as pl
from jax.experimental.pallas import tpu as pltpu
from jax.sharding import PartitionSpec as P

NT = 512
NF = 128
SPANS = (16, 48)


def make_tables(count_t, count_f):
    times = jnp.arange(count_t, dtype=jnp.int32)
    bins = count_t // 32 + jnp.arange(count_f, dtype=jnp.int32)
    phase = (times[:, None] * bins[None, :] % count_t).astype(jnp.float32) * (
        2.0 * jnp.pi / count_t
    )
    ramp = float(count_t // 16)
    tval = times.astype(jnp.float32)
    taper = jnp.minimum(jnp.minimum((tval + 0.5) / ramp, (count_t - tval - 0.5) / ramp), 1.0)
    cosine = jnp.cos(phase) * taper[:, None]
    sine = jnp.sin(phase) * taper[:, None]
    forward = jnp.stack([cosine, -sine], axis=1) / jnp.sqrt(jnp.float32(count_t))
    inverse = jnp.stack([cosine.T, -sine.T], axis=1) / jnp.sqrt(jnp.float32(count_f))
    return (forward, inverse)


def split(x):
    high = x.astype(jnp.bfloat16)
    low = (x - high.astype(jnp.float32)).astype(jnp.bfloat16)
    return high, low


def split_outside(x):
    high = lax.reduce_precision(x, exponent_bits=8, mantissa_bits=7)
    return high.astype(jnp.bfloat16), (x - high).astype(jnp.bfloat16)


def square_kernel(n_shot, n_freq, rows, cols, scale, first, y_hbm, out_ref, y_ref, sems, high, low):
    width = out_ref.shape[1] * cols
    span = out_ref.shape[3]
    j = pl.program_id(0)

    def copy(a):
        return pltpu.make_async_copy(y_hbm.at[a], y_ref.at[a], sems.at[a])

    @pl.when(j == 0)
    def _():
        for a in range(n_shot):
            copy(a).start()

        def fill(a, carry):
            copy(a).wait()
            top = pl.multiple_of(a * rows, rows)
            for b in range(n_freq):
                real = y_ref[a, b, 0]
                imag = y_ref[a, b, 1]
                for index, value in enumerate((real, imag, real + imag)):
                    h, l = split(value)
                    high[index, pl.ds(top, rows), pl.ds(b * cols, cols)] = h
                    low[index, pl.ds(top, rows), pl.ds(b * cols, cols)] = l
            return carry

        lax.fori_loop(0, n_shot, fill, 0)

    start = pl.multiple_of(j * width, width)
    block = pl.ds(start, width)
    dot = functools.partial(jnp.dot, preferred_element_type=jnp.float32)

    def product(index):
        def left(ref):
            return jnp.concatenate(
                [ref[index, pl.ds(a * rows + first, span), :] for a in range(n_shot)],
                axis=0,
            )

        lh, ll = left(high), left(low)
        rh, rl = high[index, :, block], low[index, :, block]
        return dot(lh, rh) + dot(lh, rl) + dot(ll, rh)

    rr = product(0)
    ii = product(1)
    ss = product(2)
    real = (rr - ii) * scale
    imag = (ss - rr - ii) * scale
    for a in range(n_shot):
        for b in range(out_ref.shape[1]):
            tile = (slice(a * span, (a + 1) * span), slice(b * cols, (b + 1) * cols))
            out_ref[a, b, 0] = real[tile]
            out_ref[a, b, 1] = imag[tile]


def complex_square(blocks, first, span):
    n_shot, n_freq, _, rows, cols = blocks.shape
    order = n_shot * rows
    group = 2
    kernel = functools.partial(
        square_kernel, n_shot, n_freq, rows, cols, float(-1.0 / (order ** 0.5)), first
    )
    return pl.pallas_call(
        kernel,
        out_shape=jax.ShapeDtypeStruct((n_shot, n_freq, 2, span, cols), jnp.float32),
        grid=(n_freq // group,),
        in_specs=[pl.BlockSpec(memory_space=pl.ANY)],
        out_specs=pl.BlockSpec(
            (n_shot, group, 2, span, cols), lambda j: (0, j, 0, 0, 0)
        ),
        scratch_shapes=[
            pltpu.VMEM(blocks.shape, jnp.float32),
            pltpu.SemaphoreType.DMA((n_shot,)),
            pltpu.VMEM((3, order, n_freq * cols), jnp.bfloat16),
            pltpu.VMEM((3, order, n_freq * cols), jnp.bfloat16),
        ],
        compiler_params=pltpu.CompilerParams(
            dimension_semantics=("arbitrary",), vmem_limit_bytes=60 * 1024 * 1024
        ),
    )(blocks)


def inverse_kernel(group, w_high, w_low, x_ref, out_ref):
    n_bins, parts, _, cols = x_ref.shape
    pieces = []
    for s in range(group):
        piece = x_ref[:, :, s, :].reshape(n_bins * parts, cols)
        pieces.append(piece.T)
    stacked = jnp.concatenate(pieces, axis=0)
    high, low = split(stacked)
    dot = functools.partial(jnp.dot, preferred_element_type=jnp.float32)
    total = dot(high, w_high[...]) + dot(high, w_low[...]) + dot(low, w_high[...])
    out_ref[...] = total.reshape(out_ref.shape).astype(out_ref.dtype)


def inverse_transform(home, inverse, first, total, previous):
    n_bins, _, span, cols = home.shape
    steps = inverse.shape[-1]
    table = inverse.reshape(n_bins * 2, steps)
    w_high, w_low = split_outside(table)
    group = 8
    offset = first // group
    operands = [w_high, w_low, home]
    in_specs = [
        pl.BlockSpec((n_bins * 2, steps), lambda i: (0, 0)),
        pl.BlockSpec((n_bins * 2, steps), lambda i: (0, 0)),
        pl.BlockSpec((n_bins, 2, group, cols), lambda i: (0, 0, i, 0)),
    ]
    aliases = {}
    kernel = functools.partial(inverse_kernel, group)
    if previous is not None:
        operands.append(previous)
        in_specs.append(pl.BlockSpec(memory_space=pl.ANY))
        aliases = {3: 0}
        kernel = functools.partial(inverse_kernel_into, group)
    return pl.pallas_call(
        kernel,
        out_shape=jax.ShapeDtypeStruct((total, cols, steps), jnp.bfloat16),
        grid=(span // group,),
        in_specs=in_specs,
        out_specs=pl.BlockSpec((group, cols, steps), lambda i: (i + offset, 0, 0)),
        input_output_aliases=aliases,
        compiler_params=pltpu.CompilerParams(dimension_semantics=("arbitrary",)),
    )(*operands)


def inverse_kernel_into(group, w_high, w_low, x_ref, previous_ref, out_ref):
    inverse_kernel(group, w_high, w_low, x_ref, out_ref)


def per_device(traces):
    forward, inverse = make_tables(NT, NF)
    spectra = jnp.einsum(
        "srt,tpb->bpsr",
        traces.astype(jnp.float32),
        forward,
        precision=lax.Precision.HIGH,
        preferred_element_type=jnp.float32,
    )
    rows = traces.shape[0]
    cols = traces.shape[1]
    n_shot = lax.axis_size("shot")
    n_freq = lax.axis_size("freq")
    moved = lax.all_to_all(spectra[None], ("shot", "freq"), split_axis=1, concat_axis=0, tiled=True)
    local_bins = moved.shape[-4]
    assert local_bins == 1
    blocks = moved.reshape(n_shot, n_freq, 2, rows, cols)
    result = None
    first = 0
    for span in SPANS:
        pred = complex_square(blocks, first, span)
        home = lax.all_to_all(
            pred.reshape(1, n_shot * n_freq, 2, span, cols),
            ("shot", "freq"),
            split_axis=1,
            concat_axis=0,
            tiled=True,
        )
        home = home.reshape(n_shot * n_freq, 2, span, cols)
        result = inverse_transform(home, inverse, first, rows, result)
        first += span
    assert first == rows
    return result


def solution(mesh):
    return jax.shard_map(
        per_device,
        mesh=mesh,
        in_specs=(P("shot", "freq", None),),
        out_specs=P("shot", "freq", None),
        check_vma=False,
    )
```

```python
import functools

import jax
import jax.numpy as jnp
from jax import lax
from jax.experimental import pallas as pl
from jax.experimental.pallas import tpu as pltpu
from jax.sharding import PartitionSpec as P

NT = 512
NF = 128
SPANS = (24, 40)


def make_tables(count_t, count_f):
    times = jnp.arange(count_t, dtype=jnp.int32)
    bins = count_t // 32 + jnp.arange(count_f, dtype=jnp.int32)
    phase = (times[:, None] * bins[None, :] % count_t).astype(jnp.float32) * (
        2.0 * jnp.pi / count_t
    )
    ramp = float(count_t // 16)
    tval = times.astype(jnp.float32)
    taper = jnp.minimum(jnp.minimum((tval + 0.5) / ramp, (count_t - tval - 0.5) / ramp), 1.0)
    cosine = jnp.cos(phase) * taper[:, None]
    sine = jnp.sin(phase) * taper[:, None]
    forward = jnp.stack([cosine, -sine], axis=1) / jnp.sqrt(jnp.float32(count_t))
    inverse = jnp.stack([cosine.T, -sine.T], axis=1) / jnp.sqrt(jnp.float32(count_f))
    return (forward, inverse)


def split(x):
    high = x.astype(jnp.bfloat16)
    low = (x - high.astype(jnp.float32)).astype(jnp.bfloat16)
    return high, low


def split_outside(x):
    high = lax.reduce_precision(x, exponent_bits=8, mantissa_bits=7)
    return high.astype(jnp.bfloat16), (x - high).astype(jnp.bfloat16)


def square_kernel(n_shot, n_freq, rows, cols, scale, first, y_hbm, out_ref, y_ref, sems, high, low):
    width = out_ref.shape[1] * cols
    span = out_ref.shape[3]
    j = pl.program_id(0)

    def copy(a):
        return pltpu.make_async_copy(y_hbm.at[a], y_ref.at[a], sems.at[a])

    @pl.when(j == 0)
    def _():
        for a in range(n_shot):
            copy(a).start()

        def fill(a, carry):
            copy(a).wait()
            top = pl.multiple_of(a * rows, rows)
            for b in range(n_freq):
                real = y_ref[a, b, 0]
                imag = y_ref[a, b, 1]
                for index, value in enumerate((real, imag, real + imag)):
                    h, l = split(value)
                    high[index, pl.ds(top, rows), pl.ds(b * cols, cols)] = h
                    low[index, pl.ds(top, rows), pl.ds(b * cols, cols)] = l
            return carry

        lax.fori_loop(0, n_shot, fill, 0)

    start = pl.multiple_of(j * width, width)
    block = pl.ds(start, width)
    dot = functools.partial(jnp.dot, preferred_element_type=jnp.float32)

    def product(index):
        def left(ref):
            return jnp.concatenate(
                [ref[index, pl.ds(a * rows + first, span), :] for a in range(n_shot)],
                axis=0,
            )

        lh, ll = left(high), left(low)
        rh, rl = high[index, :, block], low[index, :, block]
        return dot(lh, rh) + dot(lh, rl) + dot(ll, rh)

    rr = product(0)
    ii = product(1)
    ss = product(2)
    real = (rr - ii) * scale
    imag = (ss - rr - ii) * scale
    for a in range(n_shot):
        for b in range(out_ref.shape[1]):
            tile = (slice(a * span, (a + 1) * span), slice(b * cols, (b + 1) * cols))
            out_ref[a, b, 0] = real[tile]
            out_ref[a, b, 1] = imag[tile]


def complex_square(blocks, first, span):
    n_shot, n_freq, _, rows, cols = blocks.shape
    order = n_shot * rows
    group = 2
    kernel = functools.partial(
        square_kernel, n_shot, n_freq, rows, cols, float(-1.0 / (order ** 0.5)), first
    )
    return pl.pallas_call(
        kernel,
        out_shape=jax.ShapeDtypeStruct((n_shot, n_freq, 2, span, cols), jnp.float32),
        grid=(n_freq // group,),
        in_specs=[pl.BlockSpec(memory_space=pl.ANY)],
        out_specs=pl.BlockSpec(
            (n_shot, group, 2, span, cols), lambda j: (0, j, 0, 0, 0)
        ),
        scratch_shapes=[
            pltpu.VMEM(blocks.shape, jnp.float32),
            pltpu.SemaphoreType.DMA((n_shot,)),
            pltpu.VMEM((3, order, n_freq * cols), jnp.bfloat16),
            pltpu.VMEM((3, order, n_freq * cols), jnp.bfloat16),
        ],
        compiler_params=pltpu.CompilerParams(
            dimension_semantics=("arbitrary",), vmem_limit_bytes=60 * 1024 * 1024
        ),
    )(blocks)


def inverse_kernel(group, w_high, w_low, x_ref, out_ref):
    n_bins, parts, _, cols = x_ref.shape
    block = x_ref[...].reshape(n_bins * parts, group, cols)
    stacked = pltpu.einshape("ksr->(sr)k", block)
    high, low = split(stacked)
    dot = functools.partial(jnp.dot, preferred_element_type=jnp.float32)
    total = dot(high, w_high[...]) + dot(high, w_low[...]) + dot(low, w_high[...])
    out_ref[...] = total.reshape(out_ref.shape).astype(out_ref.dtype)


def inverse_transform(home, inverse, first, total, previous):
    n_bins, _, span, cols = home.shape
    steps = inverse.shape[-1]
    table = inverse.reshape(n_bins * 2, steps)
    w_high, w_low = split_outside(table)
    group = 8
    offset = first // group
    operands = [w_high, w_low, home]
    in_specs = [
        pl.BlockSpec((n_bins * 2, steps), lambda i: (0, 0)),
        pl.BlockSpec((n_bins * 2, steps), lambda i: (0, 0)),
        pl.BlockSpec((n_bins, 2, group, cols), lambda i: (0, 0, i, 0)),
    ]
    aliases = {}
    kernel = functools.partial(inverse_kernel, group)
    if previous is not None:
        operands.append(previous)
        in_specs.append(pl.BlockSpec(memory_space=pl.ANY))
        aliases = {3: 0}
        kernel = functools.partial(inverse_kernel_into, group)
    return pl.pallas_call(
        kernel,
        out_shape=jax.ShapeDtypeStruct((total, cols, steps), jnp.bfloat16),
        grid=(span // group,),
        in_specs=in_specs,
        out_specs=pl.BlockSpec((group, cols, steps), lambda i: (i + offset, 0, 0)),
        input_output_aliases=aliases,
        compiler_params=pltpu.CompilerParams(dimension_semantics=("arbitrary",)),
    )(*operands)


def inverse_kernel_into(group, w_high, w_low, x_ref, previous_ref, out_ref):
    inverse_kernel(group, w_high, w_low, x_ref, out_ref)


def per_device(traces):
    forward, inverse = make_tables(NT, NF)
    f_high, f_low = split_outside(forward)
    spectra = sum(
        jnp.einsum("srt,tpb->bpsr", traces, half, preferred_element_type=jnp.float32)
        for half in (f_high, f_low)
    )
    rows = traces.shape[0]
    cols = traces.shape[1]
    n_shot = lax.axis_size("shot")
    n_freq = lax.axis_size("freq")
    moved = lax.all_to_all(spectra[None], ("shot", "freq"), split_axis=1, concat_axis=0, tiled=True)
    local_bins = moved.shape[-4]
    assert local_bins == 1
    blocks = moved.reshape(n_shot, n_freq, 2, rows, cols)
    result = None
    first = 0
    for span in SPANS:
        pred = complex_square(blocks, first, span)
        home = lax.all_to_all(
            pred.reshape(1, n_shot * n_freq, 2, span, cols),
            ("shot", "freq"),
            split_axis=1,
            concat_axis=0,
            tiled=True,
        )
        home = home.reshape(n_shot * n_freq, 2, span, cols)
        result = inverse_transform(home, inverse, first, rows, result)
        first += span
    assert first == rows
    return result


def solution(mesh):
    return jax.shard_map(
        per_device,
        mesh=mesh,
        in_specs=(P("shot", "freq", None),),
        out_specs=P("shot", "freq", None),
        check_vma=False,
    )
```

```python
import functools

import jax
import jax.numpy as jnp
from jax import lax
from jax.experimental import pallas as pl
from jax.experimental.pallas import tpu as pltpu
from jax.sharding import PartitionSpec as P

NT = 512
NF = 128
SPANS = (24, 40)


def make_tables(count_t, count_f):
    times = jnp.arange(count_t, dtype=jnp.int32)
    bins = count_t // 32 + jnp.arange(count_f, dtype=jnp.int32)
    phase = (times[:, None] * bins[None, :] % count_t).astype(jnp.float32) * (
        2.0 * jnp.pi / count_t
    )
    ramp = float(count_t // 16)
    tval = times.astype(jnp.float32)
    taper = jnp.minimum(jnp.minimum((tval + 0.5) / ramp, (count_t - tval - 0.5) / ramp), 1.0)
    cosine = jnp.cos(phase) * taper[:, None]
    sine = jnp.sin(phase) * taper[:, None]
    forward = jnp.stack([cosine, -sine], axis=1) / jnp.sqrt(jnp.float32(count_t))
    inverse = jnp.stack([cosine.T, -sine.T], axis=1) / jnp.sqrt(jnp.float32(count_f))
    return (forward, inverse)


def split(x):
    high = x.astype(jnp.bfloat16)
    low = (x - high.astype(jnp.float32)).astype(jnp.bfloat16)
    return high, low


def split_outside(x):
    high = lax.reduce_precision(x, exponent_bits=8, mantissa_bits=7)
    return high.astype(jnp.bfloat16), (x - high).astype(jnp.bfloat16)


def square_kernel(n_shot, n_freq, rows, cols, scale, first, y_hbm, out_ref, y_ref, sems, high, low):
    width = out_ref.shape[1] * cols
    span = out_ref.shape[3]
    j = pl.program_id(0)

    def copy(a):
        return pltpu.make_async_copy(y_hbm.at[a], y_ref.at[a], sems.at[a])

    @pl.when(j == 0)
    def _():
        for a in range(n_shot):
            copy(a).start()

        def fill(a, carry):
            copy(a).wait()
            top = pl.multiple_of(a * rows, rows)
            for b in range(n_freq):
                real = y_ref[a, b, 0]
                imag = y_ref[a, b, 1]
                for index, value in enumerate((real, imag, real + imag)):
                    h, l = split(value)
                    high[index, pl.ds(top, rows), pl.ds(b * cols, cols)] = h
                    low[index, pl.ds(top, rows), pl.ds(b * cols, cols)] = l
            return carry

        lax.fori_loop(0, n_shot, fill, 0)

    start = pl.multiple_of(j * width, width)
    block = pl.ds(start, width)
    dot = functools.partial(jnp.dot, preferred_element_type=jnp.float32)

    def product(index):
        def left(ref):
            return jnp.concatenate(
                [ref[index, pl.ds(a * rows + first, span), :] for a in range(n_shot)],
                axis=0,
            )

        lh, ll = left(high), left(low)
        rh, rl = high[index, :, block], low[index, :, block]
        return dot(lh, rh) + dot(lh, rl) + dot(ll, rh)

    rr = product(0)
    ii = product(1)
    ss = product(2)
    real = (rr - ii) * scale
    imag = (ss - rr - ii) * scale
    for a in range(n_shot):
        for b in range(out_ref.shape[1]):
            tile = (slice(a * span, (a + 1) * span), slice(b * cols, (b + 1) * cols))
            out_ref[a, b, 0] = real[tile]
            out_ref[a, b, 1] = imag[tile]


def complex_square(blocks, first, span):
    n_shot, n_freq, _, rows, cols = blocks.shape
    order = n_shot * rows
    group = 2
    kernel = functools.partial(
        square_kernel, n_shot, n_freq, rows, cols, float(-1.0 / (order ** 0.5)), first
    )
    return pl.pallas_call(
        kernel,
        out_shape=jax.ShapeDtypeStruct((n_shot, n_freq, 2, span, cols), jnp.float32),
        grid=(n_freq // group,),
        in_specs=[pl.BlockSpec(memory_space=pl.ANY)],
        out_specs=pl.BlockSpec(
            (n_shot, group, 2, span, cols), lambda j: (0, j, 0, 0, 0)
        ),
        scratch_shapes=[
            pltpu.VMEM(blocks.shape, jnp.float32),
            pltpu.SemaphoreType.DMA((n_shot,)),
            pltpu.VMEM((3, order, n_freq * cols), jnp.bfloat16),
            pltpu.VMEM((3, order, n_freq * cols), jnp.bfloat16),
        ],
        compiler_params=pltpu.CompilerParams(
            dimension_semantics=("arbitrary",), vmem_limit_bytes=60 * 1024 * 1024
        ),
    )(blocks)


def inverse_kernel(group, w_high, w_low, x_ref, out_ref):
    n_bins, parts, _, cols = x_ref.shape
    block = x_ref[...].reshape(n_bins * parts, group, cols)
    stacked = pltpu.einshape("ksr->(sr)k", block)
    high, low = split(stacked)
    dot = functools.partial(jnp.dot, preferred_element_type=jnp.float32)
    total = dot(high, w_high[...]) + dot(high, w_low[...]) + dot(low, w_high[...])
    out_ref[...] = total.reshape(out_ref.shape).astype(out_ref.dtype)


def inverse_transform(home, inverse, first, total, previous):
    n_bins, _, span, cols = home.shape
    steps = inverse.shape[-1]
    table = inverse.reshape(n_bins * 2, steps)
    w_high, w_low = split_outside(table)
    group = 8
    offset = first // group
    operands = [w_high, w_low, home]
    in_specs = [
        pl.BlockSpec((n_bins * 2, steps), lambda i: (0, 0)),
        pl.BlockSpec((n_bins * 2, steps), lambda i: (0, 0)),
        pl.BlockSpec((n_bins, 2, group, cols), lambda i: (0, 0, i, 0)),
    ]
    aliases = {}
    kernel = functools.partial(inverse_kernel, group)
    if previous is not None:
        operands.append(previous)
        in_specs.append(pl.BlockSpec(memory_space=pl.ANY))
        aliases = {3: 0}
        kernel = functools.partial(inverse_kernel_into, group)
    return pl.pallas_call(
        kernel,
        out_shape=jax.ShapeDtypeStruct((total, cols, steps), jnp.bfloat16),
        grid=(span // group,),
        in_specs=in_specs,
        out_specs=pl.BlockSpec((group, cols, steps), lambda i: (i + offset, 0, 0)),
        input_output_aliases=aliases,
        compiler_params=pltpu.CompilerParams(dimension_semantics=("arbitrary",)),
    )(*operands)


def inverse_kernel_into(group, w_high, w_low, x_ref, previous_ref, out_ref):
    inverse_kernel(group, w_high, w_low, x_ref, out_ref)


def per_device(traces):
    forward, inverse = make_tables(NT, NF)
    spectra = jnp.einsum(
        "srt,tpb->bpsr",
        traces.astype(jnp.float32),
        forward,
        precision=lax.Precision.HIGH,
        preferred_element_type=jnp.float32,
    )
    rows = traces.shape[0]
    cols = traces.shape[1]
    n_shot = lax.axis_size("shot")
    n_freq = lax.axis_size("freq")
    moved = lax.all_to_all(spectra[None], ("shot", "freq"), split_axis=1, concat_axis=0, tiled=True)
    local_bins = moved.shape[-4]
    assert local_bins == 1
    blocks = moved.reshape(n_shot, n_freq, 2, rows, cols)
    result = None
    first = 0
    for span in SPANS:
        pred = complex_square(blocks, first, span)
        home = lax.all_to_all(
            pred.reshape(1, n_shot * n_freq, 2, span, cols),
            ("shot", "freq"),
            split_axis=1,
            concat_axis=0,
            tiled=True,
        )
        home = home.reshape(n_shot * n_freq, 2, span, cols)
        result = inverse_transform(home, inverse, first, rows, result)
        first += span
    assert first == rows
    return result


def solution(mesh):
    return jax.shard_map(
        per_device,
        mesh=mesh,
        in_specs=(P("shot", "freq", None),),
        out_specs=P("shot", "freq", None),
        check_vma=False,
    )
```

```python
import functools

import jax
import jax.numpy as jnp
from jax import lax
from jax.experimental import pallas as pl
from jax.experimental.pallas import tpu as pltpu
from jax.sharding import PartitionSpec as P

NT = 512
NF = 128
SPANS = (24, 40)


def make_tables(count_t, count_f):
    times = jnp.arange(count_t, dtype=jnp.int32)
    bins = count_t // 32 + jnp.arange(count_f, dtype=jnp.int32)
    phase = (times[:, None] * bins[None, :] % count_t).astype(jnp.float32) * (
        2.0 * jnp.pi / count_t
    )
    ramp = float(count_t // 16)
    tval = times.astype(jnp.float32)
    taper = jnp.minimum(jnp.minimum((tval + 0.5) / ramp, (count_t - tval - 0.5) / ramp), 1.0)
    cosine = jnp.cos(phase) * taper[:, None]
    sine = jnp.sin(phase) * taper[:, None]
    forward = jnp.stack([cosine, -sine], axis=1) / jnp.sqrt(jnp.float32(count_t))
    inverse = jnp.stack([cosine.T, -sine.T], axis=1) / jnp.sqrt(jnp.float32(count_f))
    return (forward, inverse)


def split(x):
    high = x.astype(jnp.bfloat16)
    low = (x - high.astype(jnp.float32)).astype(jnp.bfloat16)
    return high, low


def split_outside(x):
    high = lax.reduce_precision(x, exponent_bits=8, mantissa_bits=7)
    return high.astype(jnp.bfloat16), (x - high).astype(jnp.bfloat16)


def square_kernel(n_shot, n_freq, rows, cols, scale, first, y_hbm, out_ref, y_ref, sems, high, low):
    width = out_ref.shape[1] * cols
    span = out_ref.shape[3]
    j = pl.program_id(0)

    def copy(a):
        return pltpu.make_async_copy(y_hbm.at[a], y_ref.at[a], sems.at[a])

    @pl.when(j == 0)
    def _():
        for a in range(n_shot):
            copy(a).start()

        def fill(a, carry):
            copy(a).wait()
            top = pl.multiple_of(a * rows, rows)
            for b in range(n_freq):
                real = y_ref[a, b, 0]
                imag = y_ref[a, b, 1]
                for index, value in enumerate((real, imag, real + imag)):
                    h, l = split(value)
                    high[index, pl.ds(top, rows), pl.ds(b * cols, cols)] = h
                    low[index, pl.ds(top, rows), pl.ds(b * cols, cols)] = l
            return carry

        lax.fori_loop(0, n_shot, fill, 0)

    start = pl.multiple_of(j * width, width)
    block = pl.ds(start, width)
    dot = functools.partial(jnp.dot, preferred_element_type=jnp.float32)

    def product(index):
        def left(ref):
            return jnp.concatenate(
                [ref[index, pl.ds(a * rows + first, span), :] for a in range(n_shot)],
                axis=0,
            )

        lh, ll = left(high), left(low)
        rh, rl = high[index, :, block], low[index, :, block]
        return dot(lh, rh) + dot(lh, rl) + dot(ll, rh)

    rr = product(0)
    ii = product(1)
    ss = product(2)
    real = (rr - ii) * scale
    imag = (ss - rr - ii) * scale
    for a in range(n_shot):
        for b in range(out_ref.shape[1]):
            tile = (slice(a * span, (a + 1) * span), slice(b * cols, (b + 1) * cols))
            out_ref[a, b, 0] = real[tile]
            out_ref[a, b, 1] = imag[tile]


def complex_square(blocks, first, span):
    n_shot, n_freq, _, rows, cols = blocks.shape
    order = n_shot * rows
    group = 4
    kernel = functools.partial(
        square_kernel, n_shot, n_freq, rows, cols, float(-1.0 / (order ** 0.5)), first
    )
    return pl.pallas_call(
        kernel,
        out_shape=jax.ShapeDtypeStruct((n_shot, n_freq, 2, span, cols), jnp.float32),
        grid=(n_freq // group,),
        in_specs=[pl.BlockSpec(memory_space=pl.ANY)],
        out_specs=pl.BlockSpec(
            (n_shot, group, 2, span, cols), lambda j: (0, j, 0, 0, 0)
        ),
        scratch_shapes=[
            pltpu.VMEM(blocks.shape, jnp.float32),
            pltpu.SemaphoreType.DMA((n_shot,)),
            pltpu.VMEM((3, order, n_freq * cols), jnp.bfloat16),
            pltpu.VMEM((3, order, n_freq * cols), jnp.bfloat16),
        ],
        compiler_params=pltpu.CompilerParams(
            dimension_semantics=("arbitrary",), vmem_limit_bytes=60 * 1024 * 1024
        ),
    )(blocks)


def inverse_kernel(group, w_high, w_low, x_ref, out_ref):
    n_bins, parts, _, cols = x_ref.shape
    block = x_ref[...].reshape(n_bins * parts, group, cols)
    stacked = pltpu.einshape("ksr->(sr)k", block)
    high, low = split(stacked)
    dot = functools.partial(jnp.dot, preferred_element_type=jnp.float32)
    total = dot(high, w_high[...]) + dot(high, w_low[...]) + dot(low, w_high[...])
    out_ref[...] = total.reshape(out_ref.shape).astype(out_ref.dtype)


def inverse_transform(home, inverse, first, total, previous):
    n_bins, _, span, cols = home.shape
    steps = inverse.shape[-1]
    table = inverse.reshape(n_bins * 2, steps)
    w_high, w_low = split_outside(table)
    group = 8
    offset = first // group
    operands = [w_high, w_low, home]
    in_specs = [
        pl.BlockSpec((n_bins * 2, steps), lambda i: (0, 0)),
        pl.BlockSpec((n_bins * 2, steps), lambda i: (0, 0)),
        pl.BlockSpec((n_bins, 2, group, cols), lambda i: (0, 0, i, 0)),
    ]
    aliases = {}
    kernel = functools.partial(inverse_kernel, group)
    if previous is not None:
        operands.append(previous)
        in_specs.append(pl.BlockSpec(memory_space=pl.ANY))
        aliases = {3: 0}
        kernel = functools.partial(inverse_kernel_into, group)
    return pl.pallas_call(
        kernel,
        out_shape=jax.ShapeDtypeStruct((total, cols, steps), jnp.bfloat16),
        grid=(span // group,),
        in_specs=in_specs,
        out_specs=pl.BlockSpec((group, cols, steps), lambda i: (i + offset, 0, 0)),
        input_output_aliases=aliases,
        compiler_params=pltpu.CompilerParams(
            dimension_semantics=("arbitrary",),
        ),
    )(*operands)


def inverse_kernel_into(group, w_high, w_low, x_ref, previous_ref, out_ref):
    inverse_kernel(group, w_high, w_low, x_ref, out_ref)


def per_device(traces):
    forward, inverse = make_tables(NT, NF)
    spectra = jnp.einsum(
        "srt,tpb->bpsr",
        traces.astype(jnp.float32),
        forward,
        precision=lax.Precision.HIGH,
        preferred_element_type=jnp.float32,
    )
    rows = traces.shape[0]
    cols = traces.shape[1]
    n_shot = lax.axis_size("shot")
    n_freq = lax.axis_size("freq")
    moved = lax.all_to_all(spectra[None], ("shot", "freq"), split_axis=1, concat_axis=0, tiled=True)
    local_bins = moved.shape[-4]
    assert local_bins == 1
    blocks = moved.reshape(n_shot, n_freq, 2, rows, cols)
    result = None
    first = 0
    for span in SPANS:
        pred = complex_square(blocks, first, span)
        home = lax.all_to_all(
            pred.reshape(1, n_shot * n_freq, 2, span, cols),
            ("shot", "freq"),
            split_axis=1,
            concat_axis=0,
            tiled=True,
        )
        home = home.reshape(n_shot * n_freq, 2, span, cols)
        result = inverse_transform(home, inverse, first, rows, result)
        first += span
    assert first == rows
    return result


def solution(mesh):
    return jax.shard_map(
        per_device,
        mesh=mesh,
        in_specs=(P("shot", "freq", None),),
        out_specs=P("shot", "freq", None),
        check_vma=False,
    )
```

```python
import functools

import jax
import jax.numpy as jnp
from jax import lax
from jax.experimental import pallas as pl
from jax.experimental.pallas import tpu as pltpu
from jax.sharding import PartitionSpec as P

NT = 512
NF = 128
SPANS = (24, 40)


def make_tables(count_t, count_f):
    times = jnp.arange(count_t, dtype=jnp.int32)
    bins = count_t // 32 + jnp.arange(count_f, dtype=jnp.int32)
    phase = (times[:, None] * bins[None, :] % count_t).astype(jnp.float32) * (
        2.0 * jnp.pi / count_t
    )
    ramp = float(count_t // 16)
    tval = times.astype(jnp.float32)
    taper = jnp.minimum(jnp.minimum((tval + 0.5) / ramp, (count_t - tval - 0.5) / ramp), 1.0)
    cosine = jnp.cos(phase) * taper[:, None]
    sine = jnp.sin(phase) * taper[:, None]
    forward = jnp.stack([cosine, -sine], axis=1) / jnp.sqrt(jnp.float32(count_t))
    inverse = jnp.stack([cosine.T, -sine.T], axis=1) / jnp.sqrt(jnp.float32(count_f))
    return (forward, inverse)


def split(x):
    high = x.astype(jnp.bfloat16)
    low = (x - high.astype(jnp.float32)).astype(jnp.bfloat16)
    return high, low


def split_outside(x):
    high = lax.reduce_precision(x, exponent_bits=8, mantissa_bits=7)
    return high.astype(jnp.bfloat16), (x - high).astype(jnp.bfloat16)


def square_kernel(n_shot, n_freq, rows, cols, scale, first, y_hbm, out_ref, y_ref, sems, high, low):
    width = out_ref.shape[1] * cols
    span = out_ref.shape[3]
    j = pl.program_id(0)

    def copy(a):
        return pltpu.make_async_copy(y_hbm.at[a], y_ref.at[a], sems.at[a])

    @pl.when(j == 0)
    def _():
        for a in range(n_shot):
            copy(a).start()

        def fill(a, carry):
            copy(a).wait()
            top = pl.multiple_of(a * rows, rows)
            for b in range(n_freq):
                real = y_ref[a, b, 0]
                imag = y_ref[a, b, 1]
                for index, value in enumerate((real, imag, real + imag)):
                    h, l = split(value)
                    high[index, pl.ds(top, rows), pl.ds(b * cols, cols)] = h
                    low[index, pl.ds(top, rows), pl.ds(b * cols, cols)] = l
            return carry

        lax.fori_loop(0, n_shot, fill, 0)

    start = pl.multiple_of(j * width, width)
    block = pl.ds(start, width)
    dot = functools.partial(jnp.dot, preferred_element_type=jnp.float32)

    def product(index):
        def left(ref):
            return jnp.concatenate(
                [ref[index, pl.ds(a * rows + first, span), :] for a in range(n_shot)],
                axis=0,
            )

        lh, ll = left(high), left(low)
        rh, rl = high[index, :, block], low[index, :, block]
        return dot(lh, rh) + dot(lh, rl) + dot(ll, rh)

    rr = product(0)
    ii = product(1)
    ss = product(2)
    real = (rr - ii) * scale
    imag = (ss - rr - ii) * scale
    for a in range(n_shot):
        for b in range(out_ref.shape[1]):
            tile = (slice(a * span, (a + 1) * span), slice(b * cols, (b + 1) * cols))
            out_ref[a, b, 0] = real[tile]
            out_ref[a, b, 1] = imag[tile]


def complex_square(blocks, first, span):
    n_shot, n_freq, _, rows, cols = blocks.shape
    order = n_shot * rows
    group = 2
    kernel = functools.partial(
        square_kernel, n_shot, n_freq, rows, cols, float(-1.0 / (order ** 0.5)), first
    )
    return pl.pallas_call(
        kernel,
        out_shape=jax.ShapeDtypeStruct((n_shot, n_freq, 2, span, cols), jnp.float32),
        grid=(n_freq // group,),
        in_specs=[pl.BlockSpec(memory_space=pl.ANY)],
        out_specs=pl.BlockSpec(
            (n_shot, group, 2, span, cols), lambda j: (0, j, 0, 0, 0)
        ),
        scratch_shapes=[
            pltpu.VMEM(blocks.shape, jnp.float32),
            pltpu.SemaphoreType.DMA((n_shot,)),
            pltpu.VMEM((3, order, n_freq * cols), jnp.bfloat16),
            pltpu.VMEM((3, order, n_freq * cols), jnp.bfloat16),
        ],
        compiler_params=pltpu.CompilerParams(
            dimension_semantics=("arbitrary",), vmem_limit_bytes=60 * 1024 * 1024
        ),
    )(blocks)


def inverse_kernel(group, w_high, w_low, x_ref, out_ref):
    n_bins, parts, _, cols = x_ref.shape
    block = x_ref[...].reshape(n_bins * parts, group, cols)
    stacked = pltpu.einshape("ksr->(sr)k", block)
    high, low = split(stacked)
    dot = functools.partial(jnp.dot, preferred_element_type=jnp.float32)
    total = dot(high, w_high[...]) + dot(high, w_low[...]) + dot(low, w_high[...])
    out_ref[...] = total.reshape(out_ref.shape).astype(out_ref.dtype)


def inverse_transform(home, inverse, first, total, previous):
    n_bins, _, span, cols = home.shape
    steps = inverse.shape[-1]
    table = inverse.reshape(n_bins * 2, steps)
    w_high, w_low = split_outside(table)
    group = 8
    offset = first // group
    operands = [w_high, w_low, home]
    in_specs = [
        pl.BlockSpec((n_bins * 2, steps), lambda i: (0, 0)),
        pl.BlockSpec((n_bins * 2, steps), lambda i: (0, 0)),
        pl.BlockSpec((n_bins, 2, group, cols), lambda i: (0, 0, i, 0)),
    ]
    aliases = {}
    kernel = functools.partial(inverse_kernel, group)
    if previous is not None:
        operands.append(previous)
        in_specs.append(pl.BlockSpec(memory_space=pl.ANY))
        aliases = {3: 0}
        kernel = functools.partial(inverse_kernel_into, group)
    return pl.pallas_call(
        kernel,
        out_shape=jax.ShapeDtypeStruct((total, cols, steps), jnp.bfloat16),
        grid=(span // group,),
        in_specs=in_specs,
        out_specs=pl.BlockSpec((group, cols, steps), lambda i: (i + offset, 0, 0)),
        input_output_aliases=aliases,
        compiler_params=pltpu.CompilerParams(dimension_semantics=("arbitrary",)),
    )(*operands)


def inverse_kernel_into(group, w_high, w_low, x_ref, previous_ref, out_ref):
    inverse_kernel(group, w_high, w_low, x_ref, out_ref)


def per_device(traces):
    _, inverse = make_tables(NT, NF)
    with jax.ensure_compile_time_eval():
        forward = make_tables(NT, NF)[0]
    spectra = jnp.einsum(
        "srt,tpb->bpsr",
        traces.astype(jnp.float32),
        forward,
        precision=lax.Precision.HIGH,
        preferred_element_type=jnp.float32,
    )
    rows = traces.shape[0]
    cols = traces.shape[1]
    n_shot = lax.axis_size("shot")
    n_freq = lax.axis_size("freq")
    moved = lax.all_to_all(spectra[None], ("shot", "freq"), split_axis=1, concat_axis=0, tiled=True)
    local_bins = moved.shape[-4]
    assert local_bins == 1
    blocks = moved.reshape(n_shot, n_freq, 2, rows, cols)
    result = None
    first = 0
    for span in SPANS:
        pred = complex_square(blocks, first, span)
        home = lax.all_to_all(
            pred.reshape(1, n_shot * n_freq, 2, span, cols),
            ("shot", "freq"),
            split_axis=1,
            concat_axis=0,
            tiled=True,
        )
        home = home.reshape(n_shot * n_freq, 2, span, cols)
        result = inverse_transform(home, inverse, first, rows, result)
        first += span
    assert first == rows
    return result


def solution(mesh):
    return jax.shard_map(
        per_device,
        mesh=mesh,
        in_specs=(P("shot", "freq", None),),
        out_specs=P("shot", "freq", None),
        check_vma=False,
    )
```

```python
import functools

import jax
import jax.numpy as jnp
from jax import lax
from jax.experimental import pallas as pl
from jax.experimental.pallas import tpu as pltpu
from jax.sharding import PartitionSpec as P

NT = 512
NF = 128
SPANS = (24, 40)


def make_tables(count_t, count_f):
    times = jnp.arange(count_t, dtype=jnp.int32)
    bins = count_t // 32 + jnp.arange(count_f, dtype=jnp.int32)
    phase = (times[:, None] * bins[None, :] % count_t).astype(jnp.float32) * (
        2.0 * jnp.pi / count_t
    )
    ramp = float(count_t // 16)
    tval = times.astype(jnp.float32)
    taper = jnp.minimum(jnp.minimum((tval + 0.5) / ramp, (count_t - tval - 0.5) / ramp), 1.0)
    cosine = jnp.cos(phase) * taper[:, None]
    sine = jnp.sin(phase) * taper[:, None]
    forward = jnp.stack([cosine, -sine], axis=1) / jnp.sqrt(jnp.float32(count_t))
    inverse = jnp.stack([cosine.T, -sine.T], axis=1) / jnp.sqrt(jnp.float32(count_f))
    return (forward, inverse)


def split(x):
    high = x.astype(jnp.bfloat16)
    low = (x - high.astype(jnp.float32)).astype(jnp.bfloat16)
    return high, low


def split_outside(x):
    high = lax.reduce_precision(x, exponent_bits=8, mantissa_bits=7)
    return high.astype(jnp.bfloat16), (x - high).astype(jnp.bfloat16)


def square_kernel(n_shot, n_freq, rows, cols, scale, first, y_hbm, out_ref, y_ref, sems, high, low):
    width = out_ref.shape[1] * cols
    span = out_ref.shape[3]
    j = pl.program_id(0)

    def copy(a):
        return pltpu.make_async_copy(y_hbm.at[a], y_ref.at[a], sems.at[a])

    @pl.when(j == 0)
    def _():
        for a in range(n_shot):
            copy(a).start()

        def fill(a, carry):
            copy(a).wait()
            top = pl.multiple_of(a * rows, rows)
            for b in range(n_freq):
                real = y_ref[a, b, 0]
                imag = y_ref[a, b, 1]
                for index, value in enumerate((real, imag, real + imag)):
                    h, l = split(value)
                    high[index, pl.ds(top, rows), pl.ds(b * cols, cols)] = h
                    low[index, pl.ds(top, rows), pl.ds(b * cols, cols)] = l
            return carry

        lax.fori_loop(0, n_shot, fill, 0)

    start = pl.multiple_of(j * width, width)
    block = pl.ds(start, width)
    dot = functools.partial(jnp.dot, preferred_element_type=jnp.float32)

    def product(index):
        def left(ref):
            return jnp.concatenate(
                [ref[index, pl.ds(a * rows + first, span), :] for a in range(n_shot)],
                axis=0,
            )

        lh, ll = left(high), left(low)
        rh, rl = high[index, :, block], low[index, :, block]
        return dot(lh, rh) + dot(lh, rl) + dot(ll, rh)

    rr = product(0)
    ii = product(1)
    ss = product(2)
    real = (rr - ii) * scale
    imag = (ss - rr - ii) * scale
    for a in range(n_shot):
        for b in range(out_ref.shape[1]):
            tile = (slice(a * span, (a + 1) * span), slice(b * cols, (b + 1) * cols))
            out_ref[a, b, 0] = real[tile]
            out_ref[a, b, 1] = imag[tile]


def complex_square(blocks, first, span):
    n_shot, n_freq, _, rows, cols = blocks.shape
    order = n_shot * rows
    group = 2
    kernel = functools.partial(
        square_kernel, n_shot, n_freq, rows, cols, float(-1.0 / (order ** 0.5)), first
    )
    return pl.pallas_call(
        kernel,
        out_shape=jax.ShapeDtypeStruct((n_shot, n_freq, 2, span, cols), jnp.float32),
        grid=(n_freq // group,),
        in_specs=[pl.BlockSpec(memory_space=pl.ANY)],
        out_specs=pl.BlockSpec(
            (n_shot, group, 2, span, cols), lambda j: (0, j, 0, 0, 0)
        ),
        scratch_shapes=[
            pltpu.VMEM(blocks.shape, jnp.float32),
            pltpu.SemaphoreType.DMA((n_shot,)),
            pltpu.VMEM((3, order, n_freq * cols), jnp.bfloat16),
            pltpu.VMEM((3, order, n_freq * cols), jnp.bfloat16),
        ],
        compiler_params=pltpu.CompilerParams(
            dimension_semantics=("arbitrary",), vmem_limit_bytes=60 * 1024 * 1024
        ),
    )(blocks)


def inverse_kernel(group, w_high, w_low, x_ref, out_ref):
    n_bins, parts, _, cols = x_ref.shape
    block = x_ref[...].reshape(n_bins * parts, group, cols)
    stacked = pltpu.einshape("ksr->(sr)k", block)
    high, low = split(stacked)
    dot = functools.partial(jnp.dot, preferred_element_type=jnp.float32)
    total = dot(high, w_high[...]) + dot(high, w_low[...]) + dot(low, w_high[...])
    out_ref[...] = total.reshape(out_ref.shape).astype(out_ref.dtype)


def inverse_transform(home, inverse, first, total, previous):
    n_bins, _, span, cols = home.shape
    steps = inverse.shape[-1]
    with jax.ensure_compile_time_eval():
        w_high, w_low = split_outside(inverse.reshape(n_bins * 2, steps))
    group = 8
    offset = first // group
    operands = [w_high, w_low, home]
    in_specs = [
        pl.BlockSpec((n_bins * 2, steps), lambda i: (0, 0)),
        pl.BlockSpec((n_bins * 2, steps), lambda i: (0, 0)),
        pl.BlockSpec((n_bins, 2, group, cols), lambda i: (0, 0, i, 0)),
    ]
    aliases = {}
    kernel = functools.partial(inverse_kernel, group)
    if previous is not None:
        operands.append(previous)
        in_specs.append(pl.BlockSpec(memory_space=pl.ANY))
        aliases = {3: 0}
        kernel = functools.partial(inverse_kernel_into, group)
    return pl.pallas_call(
        kernel,
        out_shape=jax.ShapeDtypeStruct((total, cols, steps), jnp.bfloat16),
        grid=(span // group,),
        in_specs=in_specs,
        out_specs=pl.BlockSpec((group, cols, steps), lambda i: (i + offset, 0, 0)),
        input_output_aliases=aliases,
        compiler_params=pltpu.CompilerParams(dimension_semantics=("arbitrary",)),
    )(*operands)


def inverse_kernel_into(group, w_high, w_low, x_ref, previous_ref, out_ref):
    inverse_kernel(group, w_high, w_low, x_ref, out_ref)


def per_device(traces):
    with jax.ensure_compile_time_eval():
        forward, inverse = make_tables(NT, NF)
    spectra = jnp.einsum(
        "srt,tpb->bpsr",
        traces.astype(jnp.float32),
        forward,
        precision=lax.Precision.HIGH,
        preferred_element_type=jnp.float32,
    )
    rows = traces.shape[0]
    cols = traces.shape[1]
    n_shot = lax.axis_size("shot")
    n_freq = lax.axis_size("freq")
    moved = lax.all_to_all(spectra[None], ("shot", "freq"), split_axis=1, concat_axis=0, tiled=True)
    local_bins = moved.shape[-4]
    assert local_bins == 1
    blocks = moved.reshape(n_shot, n_freq, 2, rows, cols)
    result = None
    first = 0
    for span in SPANS:
        pred = complex_square(blocks, first, span)
        home = lax.all_to_all(
            pred.reshape(1, n_shot * n_freq, 2, span, cols),
            ("shot", "freq"),
            split_axis=1,
            concat_axis=0,
            tiled=True,
        )
        home = home.reshape(n_shot * n_freq, 2, span, cols)
        result = inverse_transform(home, inverse, first, rows, result)
        first += span
    assert first == rows
    return result


def solution(mesh):
    return jax.shard_map(
        per_device,
        mesh=mesh,
        in_specs=(P("shot", "freq", None),),
        out_specs=P("shot", "freq", None),
        check_vma=False,
    )
```
